256 devices in a mesh: row: 16 (over x_lo, z), col: 16 (over x_hi, y, core).
Axes of the slice: x: 4 (x_hi: 2, x_lo: 2; x = x_hi * 2 + x_lo), y: 4, z: 8, core: 2. Of those that a mesh axis runs over, the one named last changes fastest.
Arguments:
- sp2_branch: int32 [3], replicated, may hold values from 0 to 1, as said below
- p0_occupancy: int32 [32, 32], replicated, may hold values from 0 to 1, as said below
- p1_occupancy: int32 [32, 32], replicated, may hold values from 0 to 1, as said below
- p0_columns: bfloat16 [73728, 512], P('col'), as said below
- p1_tiles: bfloat16 [3, 8192, 8192], P(None, 'row', 'col'), may hold values from -6 to 6, as said below
Outputs:
- p1_next: bfloat16 [3, 8192, 8192], P(None, 'row', 'col')
The draws below stay inside these ranges and needn't reach their ends.
Inputs may be any that keep to these rules, and one draw needn't show every extreme that they name: `sp2_branch`: both values occur among the displacements. `p0_occupancy`: symmetric; every diagonal block is 1; blocks more than 8 apart around the circle of 32 blocks are 0. `p1_occupancy`: symmetric. `p0_columns`: the strips describe one symmetric matrix: a stored entry at row u and column v equals the stored entry at row v and column u; blocks more than 8 apart around the circle are zero. `p1_tiles`: each displacement's matrix is symmetric.
All inputs are finite; a program needn't handle non-finite values.
Results may differ from the reference program's by a relative error of at most 0.001.
Values may be sent and summed in bfloat16 or wider, within the bound.
No kernel may reach another device: no remote copies, remote signals or barrier semaphores. Data moves between devices by JAX's collectives and lax.ppermute only.
A program may use at most 192 MiB of HBM per device.

```python
import jax
import jax.numpy as jnp
import numpy as np
from jax import lax

DISP = 3
BLK = 256
COLB = 2
BLOCKS = 32
ROWB = 2
HALF = 8
CW = 512
RH = 512
ORDER = 8192
STRIP = 4608
RSTRIP = 4608
N_ROW = 16
N_COL = 16


def draw_sp2_branch(key, part):
    key_first, key_rest, key_order = jax.random.split(jax.random.fold_in(key, 37), 3)
    first = jax.random.randint(key_first, (1,), 0, 2).astype(jnp.int32)
    rest = jax.random.randint(key_rest, (DISP - 2,), 0, 2).astype(jnp.int32)
    values = jnp.concatenate([first, 1 - first, rest]).astype(jnp.int32)
    order = jax.random.permutation(key_order, DISP)
    return values[order].astype(jnp.int32)


def draw_p0_columns(key, part):
    key_upper, key_diag = jax.random.split(jax.random.fold_in(key, 17))
    groups = BLOCKS // COLB
    span_rows = COLB + 2 * HALF
    upper = jax.random.normal(key_upper, (BLOCKS, HALF + 1, BLK, BLK), jnp.float32) * 0.02
    diag_vals = jax.random.uniform(key_diag, (BLOCKS, BLK), jnp.float32, 0.2, 0.8)
    group_ids = np.arange(groups)[:, None, None]
    row_ids = np.arange(span_rows)[None, :, None]
    col_ids = np.arange(COLB)[None, None, :]
    shape = (groups, span_rows, COLB)
    col_block = np.broadcast_to(group_ids * COLB + col_ids, shape)
    row_block = np.broadcast_to((group_ids * COLB - HALF + row_ids) % BLOCKS, shape)
    offset = np.broadcast_to(row_ids - HALF - col_ids, shape)
    below = upper[col_block, np.clip(offset, 0, HALF)]
    above = jnp.swapaxes(upper[row_block, np.clip(-offset, 0, HALF)], -1, -2)
    eye_table = np.eye(BLK, dtype=np.float32)
    centre = 0.5 * (below + jnp.swapaxes(below, -1, -2)) + eye_table[None, None, None] * diag_vals[col_block][:, :, :, None, :]
    off_pos = jnp.asarray(offset > 0)[:, :, :, None, None]
    off_neg = jnp.asarray(offset < 0)[:, :, :, None, None]
    inside = jnp.asarray(np.abs(offset) <= HALF)[:, :, :, None, None]
    tiles = jnp.where(off_pos, below, jnp.where(off_neg, above, centre))
    tiles = jnp.where(inside, tiles, 0.0)
    strip = tiles.transpose(0, 1, 3, 2, 4).reshape(groups * span_rows * BLK, COLB * BLK)
    return strip.astype(jnp.bfloat16)


def draw_p0_occupancy(key, part):
    bits = jax.random.randint(jax.random.fold_in(key, 23), (BLOCKS, BLOCKS), 0, 4)
    rows = jnp.arange(BLOCKS, dtype=jnp.int32)[:, None]
    cols = jnp.arange(BLOCKS, dtype=jnp.int32)[None, :]
    sym = jnp.where(rows <= cols, bits, bits.T)
    dist = jnp.minimum((rows - cols) % BLOCKS, (cols - rows) % BLOCKS)
    occupied = (sym > 0).astype(jnp.int32)
    return jnp.where(dist == 0, 1, jnp.where(dist <= HALF, occupied, 0)).astype(jnp.int32)


def draw_p1_occupancy(key, part):
    key_atom, key_bits = jax.random.split(jax.random.fold_in(key, 29))
    atom = jax.random.randint(key_atom, (), 0, BLOCKS)
    bits = jax.random.randint(key_bits, (BLOCKS, BLOCKS), 0, 2)
    rows = jnp.arange(BLOCKS, dtype=jnp.int32)[:, None]
    cols = jnp.arange(BLOCKS, dtype=jnp.int32)[None, :]
    sym = jnp.where(rows <= cols, bits, bits.T)
    ids = jnp.arange(BLOCKS, dtype=jnp.int32)
    dist = jnp.minimum((ids - atom) % BLOCKS, (atom - ids) % BLOCKS)
    near_row = (dist <= BLOCKS // 8)[:, None]
    near_col = (dist <= BLOCKS // 8)[None, :]
    return jnp.where(near_row | near_col, 1, sym).astype(jnp.int32)


def draw_p1_tiles(key, part):
    base_key = jax.random.fold_in(key, 31)
    base = jax.random.normal(base_key, (DISP, ORDER, ORDER), jnp.float32)
    sym = (base + jnp.swapaxes(base, -1, -2)) * 0.7071
    return jnp.clip(sym, -6.0, 6.0).astype(jnp.bfloat16)


def setup_inputs(seed: int = 0) -> dict:
    key_of = jax.random.split(jax.random.key(seed), 6)
    sp2_branch = draw_sp2_branch(jax.random.fold_in(key_of[5], 71), 0)
    p0_occupancy = draw_p0_occupancy(jax.random.fold_in(key_of[5], 71), 0)
    p1_occupancy = draw_p1_occupancy(jax.random.fold_in(key_of[5], 71), 0)
    p0_columns = draw_p0_columns(jax.random.fold_in(key_of[5], 71), 0)
    p1_tiles = draw_p1_tiles(jax.random.fold_in(key_of[5], 71), 0)
    return dict(sp2_branch=sp2_branch, p0_occupancy=p0_occupancy, p1_occupancy=p1_occupancy, p0_columns=p0_columns, p1_tiles=p1_tiles)


def mask_blocks(values, occupancy):
    leading = values.shape[:-2]
    row_blocks = values.shape[-2] // BLK
    col_blocks = values.shape[-1] // BLK
    shaped = values.reshape(leading + (row_blocks, BLK, col_blocks, BLK))
    weight = occupancy.astype(values.dtype)[:, None, :, None]
    return (shaped * weight).reshape(values.shape)


def reference(sp2_branch, p0_occupancy, p1_occupancy, p0_columns, p1_tiles):
    strips = p0_columns.reshape(N_COL, STRIP, CW)
    group_ids = jnp.arange(N_COL, dtype=jnp.int32)
    strip_rows = (group_ids[:, None] * COLB - HALF + jnp.arange(COLB + 2 * HALF, dtype=jnp.int32)[None, :]) % BLOCKS
    strip_cols = group_ids[:, None] * COLB + jnp.arange(COLB, dtype=jnp.int32)[None, :]
    strip_occ = p0_occupancy[strip_rows[:, :, None], strip_cols[:, None, :]]
    strips_masked = jax.vmap(mask_blocks)(strips, strip_occ)
    strips_wide = strips_masked.astype(jnp.float32)
    p1_masked = mask_blocks(p1_tiles, p1_occupancy)
    col_index = ((group_ids[:, None] * COLB - HALF) * BLK + jnp.arange(STRIP, dtype=jnp.int32)[None, :]) % ORDER

    def one_row(row_id):
        rows_now = lax.dynamic_slice_in_dim(p1_masked, (row_id * RH).astype(jnp.int32), RH, 1)
        gathered = rows_now[:, :, col_index]
        right_prod = jnp.einsum("drcs,csk->drck", gathered.astype(jnp.float32), strips_wide)
        right_prod = right_prod.reshape(DISP, RH, ORDER)
        owner_col = (row_id * ROWB) // COLB
        offset_blocks = row_id * ROWB - owner_col * COLB
        owner_strip = lax.dynamic_index_in_dim(strips_masked, owner_col.astype(jnp.int32), 0, keepdims=False)
        factor = lax.dynamic_slice(owner_strip, ((offset_blocks * BLK).astype(jnp.int32), (offset_blocks * BLK).astype(jnp.int32)), (RSTRIP, RH))
        band_rows = ((row_id * ROWB - HALF) * BLK + jnp.arange(RSTRIP, dtype=jnp.int32)) % ORDER
        picked = p1_masked[:, band_rows, :]
        left_prod = jnp.einsum("kr,dkc->drc", factor.astype(jnp.float32), picked.astype(jnp.float32))
        bracket = right_prod + left_prod
        squared = (sp2_branch == 1)[:, None, None]
        chosen = jnp.where(squared, bracket, 2.0 * rows_now.astype(jnp.float32) - bracket)
        row_occ = lax.dynamic_slice(p1_occupancy, ((row_id * ROWB).astype(jnp.int32), jnp.int32(0)), (ROWB, BLOCKS))
        return mask_blocks(chosen, row_occ).astype(jnp.bfloat16)

    stacked = lax.map(one_row, jnp.arange(N_ROW, dtype=jnp.int32))
    return stacked.transpose(1, 0, 2, 3).reshape(DISP, ORDER, ORDER)
```

```python
import jax
import jax.numpy as jnp
from jax import lax
from jax.sharding import PartitionSpec as P

BLK = 256


def shifted(array, axis, by):
    length = lax.axis_size(axis)
    return lax.ppermute(array, axis, [(i, (i + by) % length) for i in range(length)])


def mask_blocks(values, occupancy):
    leading = values.shape[:-2]
    row_blocks = values.shape[-2] // BLK
    col_blocks = values.shape[-1] // BLK
    shaped = values.reshape(leading + (row_blocks, BLK, col_blocks, BLK))
    weight = occupancy.astype(values.dtype)[:, None, :, None]
    return (shaped * weight).reshape(values.shape)


def body(sp2_branch, p0_occupancy, p1_occupancy, p0_columns, p1_tiles):
    col_count = lax.axis_size("col")
    row_count = lax.axis_size("row")
    col_width = p0_columns.shape[1]
    row_height = p1_tiles.shape[1]
    col_blocks = col_width // BLK
    row_blocks = row_height // BLK
    strip_blocks = p0_columns.shape[0] // BLK
    band_half = (strip_blocks - col_blocks) // 2
    all_blocks = col_blocks * col_count
    col_span = band_half // col_blocks
    row_at = lax.axis_index("row")
    col_at = lax.axis_index("col")
    own_occ = lax.dynamic_slice(
        p1_occupancy, (row_at * row_blocks, col_at * col_blocks), (row_blocks, col_blocks)
    )
    p1_local = mask_blocks(p1_tiles, own_occ)
    tripled = jnp.concatenate([p0_occupancy, p0_occupancy, p0_occupancy], axis=0)
    strip_occ = lax.dynamic_slice(
        tripled,
        (col_at * col_blocks - band_half + all_blocks, col_at * col_blocks),
        (strip_blocks, col_blocks),
    )
    strip_local = mask_blocks(p0_columns, strip_occ)

    tiles = []
    for e in range(-col_span, col_span + 1):
        tiles.append(p1_local if e == 0 else shifted(p1_local, "col", -e))

    pairs = [(i * col_count + j, j * col_count + i) for i in range(row_count) for j in range(col_count)]
    squared = sp2_branch == 1
    outs = []
    for d in range(p1_tiles.shape[0]):
        summed = jnp.zeros((row_height, col_width), jnp.float32)
        for k, tile in enumerate(tiles):
            factor = strip_local[k * col_width : (k + 1) * col_width, :]
            summed = summed + jnp.dot(tile[d], factor, preferred_element_type=jnp.float32)
        mirrored = lax.ppermute(summed, ("row", "col"), pairs).T
        bracket = summed + mirrored
        chosen = jnp.where(squared[d], bracket, 2.0 * p1_local[d].astype(jnp.float32) - bracket)
        outs.append(chosen)
    chosen = jnp.stack(outs)
    return mask_blocks(chosen, own_occ).astype(jnp.bfloat16)


def solution(mesh):
    in_specs = (P(), P(), P(), P("col", None), P(None, "row", "col"))
    out_specs = P(None, "row", "col")
    return jax.shard_map(body, mesh=mesh, in_specs=in_specs, out_specs=out_specs, check_vma=False)
```

```python
import jax
import jax.numpy as jnp
from jax import lax
from jax.sharding import PartitionSpec as P

BLK = 256


def mask_blocks(values, occupancy):
    leading = values.shape[:-2]
    row_blocks = values.shape[-2] // BLK
    col_blocks = values.shape[-1] // BLK
    shaped = values.reshape(leading + (row_blocks, BLK, col_blocks, BLK))
    weight = occupancy.astype(values.dtype)[:, None, :, None]
    return (shaped * weight).reshape(values.shape)


def body(sp2_branch, p0_occupancy, p1_occupancy, p0_columns, p1_tiles):
    col_count = lax.axis_size("col")
    row_count = lax.axis_size("row")
    col_width = p0_columns.shape[1]
    row_height = p1_tiles.shape[1]
    col_blocks = col_width // BLK
    row_blocks = row_height // BLK
    strip_blocks = p0_columns.shape[0] // BLK
    band_half = (strip_blocks - col_blocks) // 2
    all_blocks = col_blocks * col_count
    col_span = band_half // col_blocks
    row_at = lax.axis_index("row")
    col_at = lax.axis_index("col")
    own_occ = lax.dynamic_slice(
        p1_occupancy, (row_at * row_blocks, col_at * col_blocks), (row_blocks, col_blocks)
    )
    p1_local = mask_blocks(p1_tiles, own_occ)
    tripled = jnp.concatenate([p0_occupancy, p0_occupancy, p0_occupancy], axis=0)
    strip_occ = lax.dynamic_slice(
        tripled,
        (col_at * col_blocks - band_half + all_blocks, col_at * col_blocks),
        (strip_blocks, col_blocks),
    )
    strip_local = mask_blocks(p0_columns, strip_occ)

    sign = jnp.where(col_at % 2 == 0, -1, 1)
    fetched = []
    for k in range(col_span):
        pairs = []
        for c in range(col_count):
            src = c - 1 - k if c % 2 == 0 else c + 1 + k
            pairs.append((src % col_count, c))
        fetched.append(lax.ppermute(p1_local, "col", pairs))
    swap = [(c, c ^ 1) for c in range(col_count)]
    partner_own = lax.ppermute(p1_local, "col", swap)
    partner_fetched = [lax.ppermute(fetched[j], "col", swap) for j in range(col_span - 1)]

    tiles = [(p1_local, 0)]
    tiles += [(fetched[k], sign * (k + 1)) for k in range(col_span)]
    tiles += [(partner_own, -sign)]
    tiles += [(partner_fetched[j], -sign * (j + 2)) for j in range(col_span - 1)]
    factors = []
    for _, offset in tiles:
        start = (offset + col_span) * col_width
        factors.append(lax.dynamic_slice_in_dim(strip_local, start, col_width, 0))

    pairs = [(i * col_count + j, j * col_count + i) for i in range(row_count) for j in range(col_count)]
    squared = sp2_branch == 1
    outs = []
    for d in range(p1_tiles.shape[0]):
        summed = jnp.zeros((row_height, col_width), jnp.float32)
        for (tile, _), factor in zip(tiles, factors):
            summed = summed + jnp.dot(tile[d], factor, preferred_element_type=jnp.float32)
        mirrored = lax.ppermute(summed, ("row", "col"), pairs).T
        bracket = summed + mirrored
        chosen = jnp.where(squared[d], bracket, 2.0 * p1_local[d].astype(jnp.float32) - bracket)
        outs.append(chosen)
    chosen = jnp.stack(outs)
    return mask_blocks(chosen, own_occ).astype(jnp.bfloat16)


def solution(mesh):
    in_specs = (P(), P(), P(), P("col", None), P(None, "row", "col"))
    out_specs = P(None, "row", "col")
    return jax.shard_map(body, mesh=mesh, in_specs=in_specs, out_specs=out_specs, check_vma=False)
```

```python
import jax
import jax.numpy as jnp
from jax import lax
from jax.sharding import PartitionSpec as P

BLK = 256


def mask_blocks(values, occupancy):
    leading = values.shape[:-2]
    row_blocks = values.shape[-2] // BLK
    col_blocks = values.shape[-1] // BLK
    shaped = values.reshape(leading + (row_blocks, BLK, col_blocks, BLK))
    weight = occupancy.astype(values.dtype)[:, None, :, None]
    return (shaped * weight).reshape(values.shape)


def body(sp2_branch, p0_occupancy, p1_occupancy, p0_columns, p1_tiles):
    col_count = lax.axis_size("col")
    row_count = lax.axis_size("row")
    col_width = p0_columns.shape[1]
    row_height = p1_tiles.shape[1]
    col_blocks = col_width // BLK
    row_blocks = row_height // BLK
    strip_blocks = p0_columns.shape[0] // BLK
    band_half = (strip_blocks - col_blocks) // 2
    all_blocks = col_blocks * col_count
    col_span = band_half // col_blocks
    row_at = lax.axis_index("row")
    col_at = lax.axis_index("col")
    own_occ = lax.dynamic_slice(
        p1_occupancy, (row_at * row_blocks, col_at * col_blocks), (row_blocks, col_blocks)
    )
    p1_local = mask_blocks(p1_tiles, own_occ)
    tripled = jnp.concatenate([p0_occupancy, p0_occupancy, p0_occupancy], axis=0)
    strip_occ = lax.dynamic_slice(
        tripled,
        (col_at * col_blocks - band_half + all_blocks, col_at * col_blocks),
        (strip_blocks, col_blocks),
    )
    strip_local = mask_blocks(p0_columns, strip_occ)

    sign = jnp.where(col_at % 2 == 0, -1, 1)
    fetch_pairs = []
    for k in range(col_span):
        pairs = []
        for c in range(col_count):
            src = c - 1 - k if c % 2 == 0 else c + 1 + k
            pairs.append((src % col_count, c))
        fetch_pairs.append(pairs)
    swap = [(c, c ^ 1) for c in range(col_count)]
    offsets = [0] + [sign * (k + 1) for k in range(col_span)] + [-sign]
    offsets += [-sign * (j + 2) for j in range(col_span - 1)]
    factors = []
    for offset in offsets:
        start = (offset + col_span) * col_width
        factors.append(lax.dynamic_slice_in_dim(strip_local, start, col_width, 0))

    pairs = [(i * col_count + j, j * col_count + i) for i in range(row_count) for j in range(col_count)]
    squared = sp2_branch == 1
    outs = []
    products = []
    mirrors = []
    for d in range(p1_tiles.shape[0]):
        own = p1_local[d]
        if d >= 1:
            own = lax.optimization_barrier((own, products[d - 1]))[0]
        if d >= 2:
            own = lax.optimization_barrier((own, mirrors[d - 2]))[0]
        fetched = [lax.ppermute(own, "col", fp) for fp in fetch_pairs]
        partner_own = lax.ppermute(own, "col", swap)
        partner_fetched = [lax.ppermute(fetched[j], "col", swap) for j in range(col_span - 1)]
        tiles = [own] + fetched + [partner_own] + partner_fetched
        summed = jnp.zeros((row_height, col_width), jnp.float32)
        for tile, factor in zip(tiles, factors):
            summed = summed + jnp.dot(tile, factor, preferred_element_type=jnp.float32)
        products.append(summed)
        mirrored = lax.ppermute(summed, ("row", "col"), pairs)
        mirrors.append(mirrored)
        mirrored = mirrored.T
        bracket = summed + mirrored
        chosen = jnp.where(squared[d], bracket, 2.0 * own.astype(jnp.float32) - bracket)
        outs.append(chosen)
    chosen = jnp.stack(outs)
    return mask_blocks(chosen, own_occ).astype(jnp.bfloat16)


def solution(mesh):
    in_specs = (P(), P(), P(), P("col", None), P(None, "row", "col"))
    out_specs = P(None, "row", "col")
    return jax.shard_map(body, mesh=mesh, in_specs=in_specs, out_specs=out_specs, check_vma=False)
```

```python
import jax
import jax.numpy as jnp
from jax import lax
from jax.sharding import PartitionSpec as P

BLK = 256


def mask_blocks(values, occupancy):
    leading = values.shape[:-2]
    row_blocks = values.shape[-2] // BLK
    col_blocks = values.shape[-1] // BLK
    shaped = values.reshape(leading + (row_blocks, BLK, col_blocks, BLK))
    weight = occupancy.astype(values.dtype)[:, None, :, None]
    return (shaped * weight).reshape(values.shape)


def body(sp2_branch, p0_occupancy, p1_occupancy, p0_columns, p1_tiles):
    col_count = lax.axis_size("col")
    row_count = lax.axis_size("row")
    col_width = p0_columns.shape[1]
    row_height = p1_tiles.shape[1]
    col_blocks = col_width // BLK
    row_blocks = row_height // BLK
    strip_blocks = p0_columns.shape[0] // BLK
    band_half = (strip_blocks - col_blocks) // 2
    all_blocks = col_blocks * col_count
    col_span = band_half // col_blocks
    row_at = lax.axis_index("row")
    col_at = lax.axis_index("col")
    own_occ = lax.dynamic_slice(
        p1_occupancy, (row_at * row_blocks, col_at * col_blocks), (row_blocks, col_blocks)
    )
    p1_local = mask_blocks(p1_tiles, own_occ)
    tripled = jnp.concatenate([p0_occupancy, p0_occupancy, p0_occupancy], axis=0)
    strip_occ = lax.dynamic_slice(
        tripled,
        (col_at * col_blocks - band_half + all_blocks, col_at * col_blocks),
        (strip_blocks, col_blocks),
    )
    strip_local = mask_blocks(p0_columns, strip_occ)

    sign = jnp.where(col_at % 2 == 0, -1, 1)
    fetch_pairs = []
    for k in range(col_span):
        pairs = []
        for c in range(col_count):
            src = c - 1 - k if c % 2 == 0 else c + 1 + k
            pairs.append((src % col_count, c))
        fetch_pairs.append(pairs)
    swap = [(c, c ^ 1) for c in range(col_count)]
    offsets = [0] + [sign * (k + 1) for k in range(col_span)] + [-sign]
    offsets += [-sign * (j + 2) for j in range(col_span - 1)]
    factors = []
    for offset in offsets:
        start = (offset + col_span) * col_width
        factors.append(lax.dynamic_slice_in_dim(strip_local, start, col_width, 0))

    pairs = [(i * col_count + j, j * col_count + i) for i in range(row_count) for j in range(col_count)]
    squared = sp2_branch == 1
    outs = []
    products = []
    mirrors = []
    for d in range(p1_tiles.shape[0]):
        own = p1_local[d]
        if d >= 1:
            own = lax.optimization_barrier((own, products[d - 1]))[0]
        fetched = [lax.ppermute(own, "col", fp) for fp in fetch_pairs]
        partner_own = lax.ppermute(own, "col", swap)
        partner_fetched = [lax.ppermute(fetched[j], "col", swap) for j in range(col_span - 1)]
        tiles = [own] + fetched + [partner_own] + partner_fetched
        if d >= 1:
            tiles, mirrors[d - 1] = lax.optimization_barrier((tiles, mirrors[d - 1]))
        summed = jnp.zeros((row_height, col_width), jnp.float32)
        for tile, factor in zip(tiles, factors):
            summed = summed + jnp.dot(tile, factor, preferred_element_type=jnp.float32)
        products.append(summed)
        mirrored = lax.ppermute(summed, ("row", "col"), pairs)
        mirrors.append(mirrored)
        mirrored = mirrored.T
        bracket = summed + mirrored
        chosen = jnp.where(squared[d], bracket, 2.0 * own.astype(jnp.float32) - bracket)
        outs.append(chosen)
    chosen = jnp.stack(outs)
    return mask_blocks(chosen, own_occ).astype(jnp.bfloat16)


def solution(mesh):
    in_specs = (P(), P(), P(), P("col", None), P(None, "row", "col"))
    out_specs = P(None, "row", "col")
    return jax.shard_map(body, mesh=mesh, in_specs=in_specs, out_specs=out_specs, check_vma=False)
```

```python
import jax
import jax.numpy as jnp
from jax import lax
from jax.sharding import PartitionSpec as P

BLK = 256


def mask_blocks(values, occupancy):
    leading = values.shape[:-2]
    row_blocks = values.shape[-2] // BLK
    col_blocks = values.shape[-1] // BLK
    shaped = values.reshape(leading + (row_blocks, BLK, col_blocks, BLK))
    weight = occupancy.astype(values.dtype)[:, None, :, None]
    return (shaped * weight).reshape(values.shape)


def body(sp2_branch, p0_occupancy, p1_occupancy, p0_columns, p1_tiles):
    col_count = lax.axis_size("col")
    row_count = lax.axis_size("row")
    col_width = p0_columns.shape[1]
    row_height = p1_tiles.shape[1]
    col_blocks = col_width // BLK
    row_blocks = row_height // BLK
    strip_blocks = p0_columns.shape[0] // BLK
    band_half = (strip_blocks - col_blocks) // 2
    all_blocks = col_blocks * col_count
    col_span = band_half // col_blocks
    row_at = lax.axis_index("row")
    col_at = lax.axis_index("col")
    own_occ = lax.dynamic_slice(
        p1_occupancy, (row_at * row_blocks, col_at * col_blocks), (row_blocks, col_blocks)
    )
    p1_local = mask_blocks(p1_tiles, own_occ)
    tripled = jnp.concatenate([p0_occupancy, p0_occupancy, p0_occupancy], axis=0)
    strip_occ = lax.dynamic_slice(
        tripled,
        (col_at * col_blocks - band_half + all_blocks, col_at * col_blocks),
        (strip_blocks, col_blocks),
    )
    strip_local = mask_blocks(p0_columns, strip_occ)

    sign = jnp.where(col_at % 2 == 0, -1, 1)
    fetched = []
    for k in range(col_span):
        pairs = []
        for c in range(col_count):
            src = c - 1 - k if c % 2 == 0 else c + 1 + k
            pairs.append((src % col_count, c))
        fetched.append(lax.ppermute(p1_local, "col", pairs))
    swap = [(c, c ^ 1) for c in range(col_count)]
    partner_own = lax.ppermute(p1_local, "col", swap)
    partner_fetched = [lax.ppermute(fetched[j], "col", swap) for j in range(col_span - 1)]

    tiles = [(p1_local, 0)]
    tiles += [(fetched[k], sign * (k + 1)) for k in range(col_span)]
    tiles += [(partner_own, -sign)]
    tiles += [(partner_fetched[j], -sign * (j + 2)) for j in range(col_span - 1)]
    factors = []
    for _, offset in tiles:
        start = (offset + col_span) * col_width
        factors.append(lax.dynamic_slice_in_dim(strip_local, start, col_width, 0))

    summed_col = jnp.zeros(p1_local.shape, jnp.float32)
    for (tile, _), factor in zip(tiles, factors):
        summed_col = summed_col + jnp.einsum(
            "drc,ck->drk", tile, factor, preferred_element_type=jnp.float32
        )

    row_span = band_half // row_blocks
    owner_col = row_at * row_blocks // col_blocks
    mine = col_at == owner_col
    shared = lax.psum(jnp.where(mine, strip_local, jnp.zeros_like(strip_local)), "col")
    summed_row = jnp.zeros(p1_local.shape, jnp.float32)
    for e in range(-row_span, row_span + 1):
        if e == 0:
            incoming = p1_local
        else:
            incoming = lax.ppermute(
                p1_local, "row", [(r, (r - e) % row_count) for r in range(row_count)]
            )
        factor = shared[(e + row_span) * row_height : (e + row_span + 1) * row_height, :]
        summed_row = summed_row + jnp.einsum(
            "kr,dkc->drc", factor, incoming, preferred_element_type=jnp.float32
        )
    bracket = summed_col + summed_row
    squared = (sp2_branch == 1)[:, None, None]
    chosen = jnp.where(squared, bracket, 2.0 * p1_local.astype(jnp.float32) - bracket)
    return mask_blocks(chosen, own_occ).astype(jnp.bfloat16)


def solution(mesh):
    in_specs = (P(), P(), P(), P("col", None), P(None, "row", "col"))
    out_specs = P(None, "row", "col")
    return jax.shard_map(body, mesh=mesh, in_specs=in_specs, out_specs=out_specs, check_vma=False)
```

```python
import jax
import jax.numpy as jnp
from jax import lax
from jax.sharding import PartitionSpec as P

BLK = 256


def mask_blocks(values, occupancy):
    leading = values.shape[:-2]
    row_blocks = values.shape[-2] // BLK
    col_blocks = values.shape[-1] // BLK
    shaped = values.reshape(leading + (row_blocks, BLK, col_blocks, BLK))
    weight = occupancy.astype(values.dtype)[:, None, :, None]
    return (shaped * weight).reshape(values.shape)


def body(sp2_branch, p0_occupancy, p1_occupancy, p0_columns, p1_tiles):
    col_count = lax.axis_size("col")
    row_count = lax.axis_size("row")
    col_width = p0_columns.shape[1]
    row_height = p1_tiles.shape[1]
    col_blocks = col_width // BLK
    row_blocks = row_height // BLK
    strip_blocks = p0_columns.shape[0] // BLK
    band_half = (strip_blocks - col_blocks) // 2
    all_blocks = col_blocks * col_count
    col_span = band_half // col_blocks
    row_at = lax.axis_index("row")
    col_at = lax.axis_index("col")
    own_occ = lax.dynamic_slice(
        p1_occupancy, (row_at * row_blocks, col_at * col_blocks), (row_blocks, col_blocks)
    )
    p1_local = mask_blocks(p1_tiles, own_occ)
    tripled = jnp.concatenate([p0_occupancy, p0_occupancy, p0_occupancy], axis=0)
    strip_occ = lax.dynamic_slice(
        tripled,
        (col_at * col_blocks - band_half + all_blocks, col_at * col_blocks),
        (strip_blocks, col_blocks),
    )
    strip_local = mask_blocks(p0_columns, strip_occ)

    sign = jnp.where(col_at % 2 == 0, -1, 1)
    fetch_pairs = []
    for k in range(col_span):
        pairs = []
        for c in range(col_count):
            src = c - 1 - k if c % 2 == 0 else c + 1 + k
            pairs.append((src % col_count, c))
        fetch_pairs.append(pairs)
    swap = [(c, c ^ 1) for c in range(col_count)]
    offsets = [0] + [sign * (k + 1) for k in range(col_span)] + [-sign]
    offsets += [-sign * (j + 2) for j in range(col_span - 1)]
    factors = []
    for offset in offsets:
        start = (offset + col_span) * col_width
        factors.append(lax.dynamic_slice_in_dim(strip_local, start, col_width, 0))

    up_pairs = [(j * col_count + i, i * col_count + j) for i in range(row_count) for j in range(col_count) if j > i]
    down_pairs = [(dst, src) for src, dst in up_pairs]
    is_upper = row_at < col_at
    is_diag = row_at == col_at
    is_lower = row_at > col_at
    squared = sp2_branch == 1
    outs = []
    products = []
    mirrors = []
    returns = []
    for d in range(p1_tiles.shape[0]):
        own = p1_local[d]
        if d >= 1:
            own = lax.optimization_barrier((own, products[d - 1]))[0]
        fetched = [lax.ppermute(own, "col", fp) for fp in fetch_pairs]
        partner_own = lax.ppermute(own, "col", swap)
        partner_fetched = [lax.ppermute(fetched[j], "col", swap) for j in range(col_span - 1)]
        tiles = [own] + fetched + [partner_own] + partner_fetched
        if d >= 1:
            tiles, mirrors[d - 1] = lax.optimization_barrier((tiles, mirrors[d - 1]))
        if d >= 2:
            tiles, returns[d - 2] = lax.optimization_barrier((tiles, returns[d - 2]))
        summed = jnp.zeros((row_height, col_width), jnp.float32)
        for tile, factor in zip(tiles, factors):
            summed = summed + jnp.dot(tile, factor, preferred_element_type=jnp.float32)
        products.append(summed)
        mirrored = lax.ppermute(summed, ("row", "col"), up_pairs)
        mirrors.append(mirrored)
        if d == p1_tiles.shape[0] - 1 and d >= 1:
            mirrored, returns[d - 1] = lax.optimization_barrier((mirrored, returns[d - 1]))
        other = jnp.where(is_diag, summed, mirrored).T
        bracket = summed + other
        chosen = jnp.where(squared[d], bracket, 2.0 * own.astype(jnp.float32) - bracket)
        result = mask_blocks(chosen, own_occ).astype(jnp.bfloat16)
        returned = lax.ppermute(result, ("row", "col"), down_pairs)
        returns.append(returned)
        outs.append(jnp.where(is_lower, returned.T, result))
    return jnp.stack(outs)


def solution(mesh):
    in_specs = (P(), P(), P(), P("col", None), P(None, "row", "col"))
    out_specs = P(None, "row", "col")
    return jax.shard_map(body, mesh=mesh, in_specs=in_specs, out_specs=out_specs, check_vma=False)
```

```python
import jax
import jax.numpy as jnp
from jax import lax
from jax.sharding import PartitionSpec as P

BLK = 256


def mask_blocks(values, occupancy):
    leading = values.shape[:-2]
    row_blocks = values.shape[-2] // BLK
    col_blocks = values.shape[-1] // BLK
    shaped = values.reshape(leading + (row_blocks, BLK, col_blocks, BLK))
    weight = occupancy.astype(values.dtype)[:, None, :, None]
    return (shaped * weight).reshape(values.shape)


def body(sp2_branch, p0_occupancy, p1_occupancy, p0_columns, p1_tiles):
    col_count = lax.axis_size("col")
    row_count = lax.axis_size("row")
    col_width = p0_columns.shape[1]
    row_height = p1_tiles.shape[1]
    col_blocks = col_width // BLK
    row_blocks = row_height // BLK
    strip_blocks = p0_columns.shape[0] // BLK
    band_half = (strip_blocks - col_blocks) // 2
    all_blocks = col_blocks * col_count
    col_span = band_half // col_blocks
    row_at = lax.axis_index("row")
    col_at = lax.axis_index("col")
    own_occ = lax.dynamic_slice(
        p1_occupancy, (row_at * row_blocks, col_at * col_blocks), (row_blocks, col_blocks)
    )
    p1_local = mask_blocks(p1_tiles, own_occ)
    tripled = jnp.concatenate([p0_occupancy, p0_occupancy, p0_occupancy], axis=0)
    strip_occ = lax.dynamic_slice(
        tripled,
        (col_at * col_blocks - band_half + all_blocks, col_at * col_blocks),
        (strip_blocks, col_blocks),
    )
    strip_local = mask_blocks(p0_columns, strip_occ)

    sign = jnp.where(col_at % 2 == 0, -1, 1)
    fetch_pairs = []
    for k in range(col_span):
        pairs = []
        for c in range(col_count):
            src = c - 1 - k if c % 2 == 0 else c + 1 + k
            pairs.append((src % col_count, c))
        fetch_pairs.append(pairs)
    swap = [(c, c ^ 1) for c in range(col_count)]
    offsets = [0] + [sign * (k + 1) for k in range(col_span)] + [-sign]
    offsets += [-sign * (j + 2) for j in range(col_span - 1)]
    factors = []
    for offset in offsets:
        start = (offset + col_span) * col_width
        factors.append(lax.dynamic_slice_in_dim(strip_local, start, col_width, 0))

    pairs = [(i * col_count + j, j * col_count + i) for i in range(row_count) for j in range(col_count)]
    squared = sp2_branch == 1
    row_span = band_half // row_blocks
    owner_col = row_at * row_blocks // col_blocks
    shared = lax.psum(jnp.where(col_at == owner_col, strip_local, jnp.zeros_like(strip_local)), "col")
    first_left = jnp.zeros((row_height, col_width), jnp.float32)
    for e in range(-row_span, row_span + 1):
        if e == 0:
            incoming = p1_local[0]
        else:
            incoming = lax.ppermute(
                p1_local[0], "row", [(r, (r - e) % row_count) for r in range(row_count)]
            )
        factor = shared[(e + row_span) * row_height : (e + row_span + 1) * row_height, :]
        first_left = first_left + jnp.dot(factor.T, incoming, preferred_element_type=jnp.float32)

    outs = []
    products = []
    mirrors = []
    for d in range(p1_tiles.shape[0]):
        own = p1_local[d]
        if d >= 2:
            own = lax.optimization_barrier((own, products[d - 1]))[0]
        fetched = [lax.ppermute(own, "col", fp) for fp in fetch_pairs]
        partner_own = lax.ppermute(own, "col", swap)
        partner_fetched = [lax.ppermute(fetched[j], "col", swap) for j in range(col_span - 1)]
        tiles = [own] + fetched + [partner_own] + partner_fetched
        if d == 1:
            tiles, first_left, products[0] = lax.optimization_barrier((tiles, first_left, products[0]))
        if d >= 2:
            tiles, mirrors[d - 1] = lax.optimization_barrier((tiles, mirrors[d - 1]))
        summed = jnp.zeros((row_height, col_width), jnp.float32)
        for tile, factor in zip(tiles, factors):
            summed = summed + jnp.dot(tile, factor, preferred_element_type=jnp.float32)
        products.append(summed)
        if d == 0:
            mirrors.append(None)
            bracket = summed + first_left
        else:
            mirrored = lax.ppermute(summed, ("row", "col"), pairs)
            mirrors.append(mirrored)
            bracket = summed + mirrored.T
        chosen = jnp.where(squared[d], bracket, 2.0 * own.astype(jnp.float32) - bracket)
        outs.append(chosen)
    chosen = jnp.stack(outs)
    return mask_blocks(chosen, own_occ).astype(jnp.bfloat16)


def solution(mesh):
    in_specs = (P(), P(), P(), P("col", None), P(None, "row", "col"))
    out_specs = P(None, "row", "col")
    return jax.shard_map(body, mesh=mesh, in_specs=in_specs, out_specs=out_specs, check_vma=False)
```

```python
import jax
import jax.numpy as jnp
from jax import lax
from jax.sharding import PartitionSpec as P

BLK = 256


def mask_blocks(values, occupancy):
    leading = values.shape[:-2]
    row_blocks = values.shape[-2] // BLK
    col_blocks = values.shape[-1] // BLK
    shaped = values.reshape(leading + (row_blocks, BLK, col_blocks, BLK))
    weight = occupancy.astype(values.dtype)[:, None, :, None]
    return (shaped * weight).reshape(values.shape)


def body(sp2_branch, p0_occupancy, p1_occupancy, p0_columns, p1_tiles):
    col_count = lax.axis_size("col")
    row_count = lax.axis_size("row")
    col_width = p0_columns.shape[1]
    row_height = p1_tiles.shape[1]
    col_blocks = col_width // BLK
    row_blocks = row_height // BLK
    strip_blocks = p0_columns.shape[0] // BLK
    band_half = (strip_blocks - col_blocks) // 2
    all_blocks = col_blocks * col_count
    col_span = band_half // col_blocks
    row_at = lax.axis_index("row")
    col_at = lax.axis_index("col")
    own_occ = lax.dynamic_slice(
        p1_occupancy, (row_at * row_blocks, col_at * col_blocks), (row_blocks, col_blocks)
    )
    p1_local = mask_blocks(p1_tiles, own_occ)
    tripled = jnp.concatenate([p0_occupancy, p0_occupancy, p0_occupancy], axis=0)
    strip_occ = lax.dynamic_slice(
        tripled,
        (col_at * col_blocks - band_half + all_blocks, col_at * col_blocks),
        (strip_blocks, col_blocks),
    )
    strip_local = mask_blocks(p0_columns, strip_occ)

    sign = jnp.where(col_at % 2 == 0, -1, 1)
    fetch_pairs = []
    for k in range(col_span):
        pairs = []
        for c in range(col_count):
            src = c - 1 - k if c % 2 == 0 else c + 1 + k
            pairs.append((src % col_count, c))
        fetch_pairs.append(pairs)
    swap = [(c, c ^ 1) for c in range(col_count)]
    offsets = [0] + [sign * (k + 1) for k in range(col_span)] + [-sign]
    offsets += [-sign * (j + 2) for j in range(col_span - 1)]
    factors = []
    for offset in offsets:
        start = (offset + col_span) * col_width
        factors.append(lax.dynamic_slice_in_dim(strip_local, start, col_width, 0))

    band_factor = jnp.concatenate(factors, axis=0)

    pairs = [(i * col_count + j, j * col_count + i) for i in range(row_count) for j in range(col_count)]
    squared = sp2_branch == 1
    outs = []
    products = []
    mirrors = []
    for d in range(p1_tiles.shape[0]):
        own = p1_local[d]
        if d >= 1:
            own = lax.optimization_barrier((own, products[d - 1]))[0]
        fetched = [lax.ppermute(own, "col", fp) for fp in fetch_pairs]
        partner_own = lax.ppermute(own, "col", swap)
        partner_fetched = [lax.ppermute(fetched[j], "col", swap) for j in range(col_span - 1)]
        tiles = [own] + fetched + [partner_own] + partner_fetched
        if d >= 1:
            tiles, mirrors[d - 1] = lax.optimization_barrier((tiles, mirrors[d - 1]))
        summed = jnp.dot(
            jnp.concatenate(tiles, axis=1), band_factor, preferred_element_type=jnp.float32
        )
        products.append(summed)
        mirrored = lax.ppermute(summed, ("row", "col"), pairs)
        mirrors.append(mirrored)
        mirrored = mirrored.T
        bracket = summed + mirrored
        chosen = jnp.where(squared[d], bracket, 2.0 * own.astype(jnp.float32) - bracket)
        outs.append(chosen)
    chosen = jnp.stack(outs)
    return mask_blocks(chosen, own_occ).astype(jnp.bfloat16)


def solution(mesh):
    in_specs = (P(), P(), P(), P("col", None), P(None, "row", "col"))
    out_specs = P(None, "row", "col")
    return jax.shard_map(body, mesh=mesh, in_specs=in_specs, out_specs=out_specs, check_vma=False)
```

```python
import jax
import jax.numpy as jnp
from jax import lax
from jax.sharding import PartitionSpec as P

BLK = 256


def mask_blocks(values, occupancy):
    leading = values.shape[:-2]
    row_blocks = values.shape[-2] // BLK
    col_blocks = values.shape[-1] // BLK
    shaped = values.reshape(leading + (row_blocks, BLK, col_blocks, BLK))
    weight = occupancy.astype(values.dtype)[:, None, :, None]
    return (shaped * weight).reshape(values.shape)


def body(sp2_branch, p0_occupancy, p1_occupancy, p0_columns, p1_tiles):
    col_count = lax.axis_size("col")
    row_count = lax.axis_size("row")
    col_width = p0_columns.shape[1]
    row_height = p1_tiles.shape[1]
    col_blocks = col_width // BLK
    row_blocks = row_height // BLK
    strip_blocks = p0_columns.shape[0] // BLK
    band_half = (strip_blocks - col_blocks) // 2
    all_blocks = col_blocks * col_count
    col_span = band_half // col_blocks
    row_at = lax.axis_index("row")
    col_at = lax.axis_index("col")
    own_occ = lax.dynamic_slice(
        p1_occupancy, (row_at * row_blocks, col_at * col_blocks), (row_blocks, col_blocks)
    )
    p1_local = mask_blocks(p1_tiles, own_occ)
    tripled = jnp.concatenate([p0_occupancy, p0_occupancy, p0_occupancy], axis=0)
    strip_occ = lax.dynamic_slice(
        tripled,
        (col_at * col_blocks - band_half + all_blocks, col_at * col_blocks),
        (strip_blocks, col_blocks),
    )
    strip_local = mask_blocks(p0_columns, strip_occ)

    sign = jnp.where(col_at % 2 == 0, -1, 1)
    fetch_pairs = []
    for k in range(col_span):
        pairs = []
        for c in range(col_count):
            src = c - 1 - k if c % 2 == 0 else c + 1 + k
            pairs.append((src % col_count, c))
        fetch_pairs.append(pairs)
    swap = [(c, c ^ 1) for c in range(col_count)]
    offsets = [0] + [sign * (k + 1) for k in range(col_span)] + [-sign]
    offsets += [-sign * (j + 2) for j in range(col_span - 1)]
    factors = []
    for offset in offsets:
        start = (offset + col_span) * col_width
        factors.append(lax.dynamic_slice_in_dim(strip_local, start, col_width, 0))

    pairs = [(i * col_count + j, j * col_count + i) for i in range(row_count) for j in range(col_count)]
    squared = sp2_branch == 1
    outs = []
    products = []
    mirrors = []
    for d in range(p1_tiles.shape[0]):
        own = p1_local[d]
        if d >= 1:
            own = lax.optimization_barrier((own, products[0]))[0]
        fetched = [lax.ppermute(own, "col", fp) for fp in fetch_pairs]
        partner_own = lax.ppermute(own, "col", swap)
        partner_fetched = [lax.ppermute(fetched[j], "col", swap) for j in range(col_span - 1)]
        tiles = [own] + fetched + [partner_own] + partner_fetched
        if d >= 1:
            tiles, mirrors[d - 1] = lax.optimization_barrier((tiles, mirrors[d - 1]))
        summed = jnp.zeros((row_height, col_width), jnp.float32)
        for tile, factor in zip(tiles, factors):
            summed = summed + jnp.dot(tile, factor, preferred_element_type=jnp.float32)
        products.append(summed)
        mirrored = lax.ppermute(summed, ("row", "col"), pairs)
        mirrors.append(mirrored)
        mirrored = mirrored.T
        bracket = summed + mirrored
        chosen = jnp.where(squared[d], bracket, 2.0 * own.astype(jnp.float32) - bracket)
        outs.append(chosen)
    chosen = jnp.stack(outs)
    return mask_blocks(chosen, own_occ).astype(jnp.bfloat16)


def solution(mesh):
    in_specs = (P(), P(), P(), P("col", None), P(None, "row", "col"))
    out_specs = P(None, "row", "col")
    return jax.shard_map(body, mesh=mesh, in_specs=in_specs, out_specs=out_specs, check_vma=False)
```

```python
import jax
import jax.numpy as jnp
from jax import lax
from jax.sharding import PartitionSpec as P

BLK = 256


def mask_blocks(values, occupancy):
    leading = values.shape[:-2]
    row_blocks = values.shape[-2] // BLK
    col_blocks = values.shape[-1] // BLK
    shaped = values.reshape(leading + (row_blocks, BLK, col_blocks, BLK))
    weight = occupancy.astype(values.dtype)[:, None, :, None]
    return (shaped * weight).reshape(values.shape)


def body(sp2_branch, p0_occupancy, p1_occupancy, p0_columns, p1_tiles):
    col_count = lax.axis_size("col")
    row_count = lax.axis_size("row")
    col_width = p0_columns.shape[1]
    row_height = p1_tiles.shape[1]
    col_blocks = col_width // BLK
    row_blocks = row_height // BLK
    strip_blocks = p0_columns.shape[0] // BLK
    band_half = (strip_blocks - col_blocks) // 2
    all_blocks = col_blocks * col_count
    col_span = band_half // col_blocks
    row_at = lax.axis_index("row")
    col_at = lax.axis_index("col")
    own_occ = lax.dynamic_slice(
        p1_occupancy, (row_at * row_blocks, col_at * col_blocks), (row_blocks, col_blocks)
    )
    p1_local = mask_blocks(p1_tiles, own_occ)
    tripled = jnp.concatenate([p0_occupancy, p0_occupancy, p0_occupancy], axis=0)
    strip_occ = lax.dynamic_slice(
        tripled,
        (col_at * col_blocks - band_half + all_blocks, col_at * col_blocks),
        (strip_blocks, col_blocks),
    )
    strip_local = mask_blocks(p0_columns, strip_occ)

    sign = jnp.where(col_at % 2 == 0, -1, 1)
    fetch_pairs = []
    for k in range(col_span):
        pairs = []
        for c in range(col_count):
            src = c - 1 - k if c % 2 == 0 else c + 1 + k
            pairs.append((src % col_count, c))
        fetch_pairs.append(pairs)
    swap = [(c, c ^ 1) for c in range(col_count)]
    offsets = [0] + [sign * (k + 1) for k in range(col_span)] + [-sign]
    offsets += [-sign * (j + 2) for j in range(col_span - 1)]
    factors = []
    for offset in offsets:
        start = (offset + col_span) * col_width
        factors.append(lax.dynamic_slice_in_dim(strip_local, start, col_width, 0))

    pairs = [(i * col_count + j, j * col_count + i) for i in range(row_count) for j in range(col_count)]
    squared = sp2_branch == 1
    outs = []
    products = []
    mirrors = []
    def tile_occ(offset):
        src_col = (col_at + offset) % col_count
        return lax.dynamic_slice(p1_occupancy, (row_at * row_blocks, src_col * col_blocks), (row_blocks, col_blocks))

    occs = [tile_occ(offset) for offset in offsets]
    for d in range(p1_tiles.shape[0]):
        own = p1_tiles[d]
        if d >= 1:
            own = lax.optimization_barrier((own, products[d - 1]))[0]
        fetched = [lax.ppermute(own, "col", fp) for fp in fetch_pairs]
        partner_own = lax.ppermute(own, "col", swap)
        partner_fetched = [lax.ppermute(fetched[j], "col", swap) for j in range(col_span - 1)]
        tiles = [own] + fetched + [partner_own] + partner_fetched
        tiles = [mask_blocks(tile, occ) for tile, occ in zip(tiles, occs)]
        if d >= 1:
            tiles, mirrors[d - 1] = lax.optimization_barrier((tiles, mirrors[d - 1]))
        summed = jnp.zeros((row_height, col_width), jnp.float32)
        for tile, factor in zip(tiles, factors):
            summed = summed + jnp.dot(tile, factor, preferred_element_type=jnp.float32)
        products.append(summed)
        mirrored = lax.ppermute(summed, ("row", "col"), pairs)
        mirrors.append(mirrored)
        ahead = jnp.where(squared[d], summed, 2.0 * p1_local[d].astype(jnp.float32) - summed)
        sgn = jnp.where(squared[d], 1.0, -1.0).astype(jnp.float32)
        chosen = ahead + sgn * mirrored.T
        outs.append(chosen)
    chosen = jnp.stack(outs)
    return mask_blocks(chosen, own_occ).astype(jnp.bfloat16)


def solution(mesh):
    in_specs = (P(), P(), P(), P("col", None), P(None, "row", "col"))
    out_specs = P(None, "row", "col")
    return jax.shard_map(body, mesh=mesh, in_specs=in_specs, out_specs=out_specs, check_vma=False)
```

```python
import jax
import jax.numpy as jnp
from jax import lax
from jax.sharding import PartitionSpec as P

BLK = 256


def mask_blocks(values, occupancy):
    leading = values.shape[:-2]
    row_blocks = values.shape[-2] // BLK
    col_blocks = values.shape[-1] // BLK
    shaped = values.reshape(leading + (row_blocks, BLK, col_blocks, BLK))
    weight = occupancy.astype(values.dtype)[:, None, :, None]
    return (shaped * weight).reshape(values.shape)


def body(sp2_branch, p0_occupancy, p1_occupancy, p0_columns, p1_tiles):
    col_count = lax.axis_size("col")
    row_count = lax.axis_size("row")
    col_width = p0_columns.shape[1]
    row_height = p1_tiles.shape[1]
    col_blocks = col_width // BLK
    row_blocks = row_height // BLK
    strip_blocks = p0_columns.shape[0] // BLK
    band_half = (strip_blocks - col_blocks) // 2
    all_blocks = col_blocks * col_count
    col_span = band_half // col_blocks
    row_at = lax.axis_index("row")
    col_at = lax.axis_index("col")
    own_occ = lax.dynamic_slice(
        p1_occupancy, (row_at * row_blocks, col_at * col_blocks), (row_blocks, col_blocks)
    )
    p1_local = mask_blocks(p1_tiles, own_occ)
    tripled = jnp.concatenate([p0_occupancy, p0_occupancy, p0_occupancy], axis=0)
    strip_occ = lax.dynamic_slice(
        tripled,
        (col_at * col_blocks - band_half + all_blocks, col_at * col_blocks),
        (strip_blocks, col_blocks),
    )
    strip_local = mask_blocks(p0_columns, strip_occ)

    sign = jnp.where(col_at % 2 == 0, -1, 1)
    fetch_pairs = []
    for k in range(col_span):
        pairs = []
        for c in range(col_count):
            src = c - 1 - k if c % 2 == 0 else c + 1 + k
            pairs.append((src % col_count, c))
        fetch_pairs.append(pairs)
    swap = [(c, c ^ 1) for c in range(col_count)]
    offsets = [0] + [sign * (k + 1) for k in range(col_span)] + [-sign]
    offsets += [-sign * (j + 2) for j in range(col_span - 1)]
    factors = []
    for offset in offsets:
        start = (offset + col_span) * col_width
        factors.append(lax.dynamic_slice_in_dim(strip_local, start, col_width, 0))

    pairs = [(i * col_count + j, j * col_count + i) for i in range(row_count) for j in range(col_count)]
    squared = sp2_branch == 1
    outs = []
    products = []
    mirrors = []
    band_cols = (col_at + jnp.arange(-col_span, col_span + 1)) % col_count
    for d in range(p1_tiles.shape[0]):
        own = p1_local[d]
        if d >= 1:
            own = lax.optimization_barrier((own, products[d - 1]))[0]
        everyone = lax.all_gather(own, "col", axis=0)
        if d >= 1:
            everyone, mirrors[d - 1] = lax.optimization_barrier((everyone, mirrors[d - 1]))
        band = jnp.take(everyone, band_cols, axis=0)
        band = jnp.transpose(band, (1, 0, 2)).reshape(row_height, -1)
        summed = jnp.dot(band, strip_local, preferred_element_type=jnp.float32)
        products.append(summed)
        mirrored = lax.ppermute(summed, ("row", "col"), pairs)
        mirrors.append(mirrored)
        mirrored = mirrored.T
        bracket = summed + mirrored
        chosen = jnp.where(squared[d], bracket, 2.0 * own.astype(jnp.float32) - bracket)
        outs.append(chosen)
    chosen = jnp.stack(outs)
    return mask_blocks(chosen, own_occ).astype(jnp.bfloat16)


def solution(mesh):
    in_specs = (P(), P(), P(), P("col", None), P(None, "row", "col"))
    out_specs = P(None, "row", "col")
    return jax.shard_map(body, mesh=mesh, in_specs=in_specs, out_specs=out_specs, check_vma=False)
```

```python
import jax
import jax.numpy as jnp
from jax import lax
from jax.sharding import PartitionSpec as P

BLK = 256


def mask_blocks(values, occupancy):
    leading = values.shape[:-2]
    row_blocks = values.shape[-2] // BLK
    col_blocks = values.shape[-1] // BLK
    shaped = values.reshape(leading + (row_blocks, BLK, col_blocks, BLK))
    weight = occupancy.astype(values.dtype)[:, None, :, None]
    return (shaped * weight).reshape(values.shape)


def body(sp2_branch, p0_occupancy, p1_occupancy, p0_columns, p1_tiles):
    col_count = lax.axis_size("col")
    row_count = lax.axis_size("row")
    col_width = p0_columns.shape[1]
    row_height = p1_tiles.shape[1]
    col_blocks = col_width // BLK
    row_blocks = row_height // BLK
    strip_blocks = p0_columns.shape[0] // BLK
    band_half = (strip_blocks - col_blocks) // 2
    all_blocks = col_blocks * col_count
    col_span = band_half // col_blocks
    row_at = lax.axis_index("row")
    col_at = lax.axis_index("col")
    own_occ = lax.dynamic_slice(
        p1_occupancy, (row_at * row_blocks, col_at * col_blocks), (row_blocks, col_blocks)
    )
    p1_local = mask_blocks(p1_tiles, own_occ)
    tripled = jnp.concatenate([p0_occupancy, p0_occupancy, p0_occupancy], axis=0)
    strip_occ = lax.dynamic_slice(
        tripled,
        (col_at * col_blocks - band_half + all_blocks, col_at * col_blocks),
        (strip_blocks, col_blocks),
    )
    strip_local = mask_blocks(p0_columns, strip_occ)

    sign = jnp.where(col_at % 2 == 0, -1, 1)
    fetch_pairs = []
    for k in range(col_span):
        pairs = []
        for c in range(col_count):
            src = c - 1 - k if c % 2 == 0 else c + 1 + k
            pairs.append((src % col_count, c))
        fetch_pairs.append(pairs)
    swap = [(c, c ^ 1) for c in range(col_count)]
    offsets = [0] + [sign * (k + 1) for k in range(col_span)] + [-sign]
    offsets += [-sign * (j + 2) for j in range(col_span - 1)]
    factors = []
    for offset in offsets:
        start = (offset + col_span) * col_width
        factors.append(lax.dynamic_slice_in_dim(strip_local, start, col_width, 0))

    pairs = [(i * col_count + j, j * col_count + i) for i in range(row_count) for j in range(col_count)]
    squared = sp2_branch == 1
    def gather_tiles(own):
        fetched = [lax.ppermute(own, "col", fp) for fp in fetch_pairs]
        partner_own = lax.ppermute(own, "col", swap)
        partner_fetched = [lax.ppermute(fetched[j], "col", swap) for j in range(col_span - 1)]
        return [own] + fetched + [partner_own] + partner_fetched

    def product(tiles):
        summed = jnp.zeros((row_height, col_width), jnp.float32)
        for tile, factor in zip(tiles, factors):
            summed = summed + jnp.dot(tile, factor, preferred_element_type=jnp.float32)
        return summed

    disp = p1_tiles.shape[0]
    products = [product(gather_tiles(p1_local[0]))]
    mirrors = [lax.ppermute(products[0], ("row", "col"), pairs)]
    later = lax.optimization_barrier((p1_local[1:], products[0]))[0]
    later_tiles = [gather_tiles(later[d]) for d in range(disp - 1)]
    later_tiles, mirrors[0] = lax.optimization_barrier((later_tiles, mirrors[0]))
    for tiles in later_tiles:
        products.append(product(tiles))
        mirrors.append(lax.ppermute(products[-1], ("row", "col"), pairs))
    outs = []
    for d in range(disp):
        bracket = products[d] + mirrors[d].T
        chosen = jnp.where(squared[d], bracket, 2.0 * p1_local[d].astype(jnp.float32) - bracket)
        outs.append(chosen)
    chosen = jnp.stack(outs)
    return mask_blocks(chosen, own_occ).astype(jnp.bfloat16)


def solution(mesh):
    in_specs = (P(), P(), P(), P("col", None), P(None, "row", "col"))
    out_specs = P(None, "row", "col")
    return jax.shard_map(body, mesh=mesh, in_specs=in_specs, out_specs=out_specs, check_vma=False)
```

```python
import jax
import jax.numpy as jnp
from jax import lax
from jax.sharding import PartitionSpec as P

BLK = 256


def mask_blocks(values, occupancy):
    leading = values.shape[:-2]
    row_blocks = values.shape[-2] // BLK
    col_blocks = values.shape[-1] // BLK
    shaped = values.reshape(leading + (row_blocks, BLK, col_blocks, BLK))
    weight = occupancy.astype(values.dtype)[:, None, :, None]
    return (shaped * weight).reshape(values.shape)


def body(sp2_branch, p0_occupancy, p1_occupancy, p0_columns, p1_tiles):
    col_count = lax.axis_size("col")
    row_count = lax.axis_size("row")
    col_width = p0_columns.shape[1]
    row_height = p1_tiles.shape[1]
    col_blocks = col_width // BLK
    row_blocks = row_height // BLK
    strip_blocks = p0_columns.shape[0] // BLK
    band_half = (strip_blocks - col_blocks) // 2
    all_blocks = col_blocks * col_count
    col_span = band_half // col_blocks
    row_at = lax.axis_index("row")
    col_at = lax.axis_index("col")
    own_occ = lax.dynamic_slice(
        p1_occupancy, (row_at * row_blocks, col_at * col_blocks), (row_blocks, col_blocks)
    )
    p1_local = mask_blocks(p1_tiles, own_occ)
    tripled = jnp.concatenate([p0_occupancy, p0_occupancy, p0_occupancy], axis=0)
    strip_occ = lax.dynamic_slice(
        tripled,
        (col_at * col_blocks - band_half + all_blocks, col_at * col_blocks),
        (strip_blocks, col_blocks),
    )
    strip_local = mask_blocks(p0_columns, strip_occ)

    sign = jnp.where(col_at % 2 == 0, -1, 1)
    fetch_pairs = []
    for k in range(col_span):
        pairs = []
        for c in range(col_count):
            src = c - 1 - k if c % 2 == 0 else c + 1 + k
            pairs.append((src % col_count, c))
        fetch_pairs.append(pairs)
    swap = [(c, c ^ 1) for c in range(col_count)]
    offsets = [0] + [sign * (k + 1) for k in range(col_span)] + [-sign]
    offsets += [-sign * (j + 2) for j in range(col_span - 1)]
    factors = []
    for offset in offsets:
        start = (offset + col_span) * col_width
        factors.append(lax.dynamic_slice_in_dim(strip_local, start, col_width, 0))

    pairs = [(i * col_count + j, j * col_count + i) for i in range(row_count) for j in range(col_count)]
    squared = sp2_branch == 1
    outs = []
    products = []
    mirrors = []
    for d in range(p1_tiles.shape[0]):
        own = p1_local[d]
        if d >= 1:
            own = lax.optimization_barrier((own, products[d - 1]))[0]
        near = [lax.ppermute(own, "col", fp) for fp in fetch_pairs[:2]]
        relay = [(c, (c + 2) % col_count) if c % 2 == 0 else (c, (c - 2) % col_count) for c in range(col_count)]
        far = lax.ppermute(jnp.stack(near, axis=0), "col", relay)
        fetched = near + [far[0], far[1]]
        partner_own = lax.ppermute(own, "col", swap)
        partner_fetched = [lax.ppermute(fetched[j], "col", swap) for j in range(col_span - 1)]
        tiles = [own] + fetched + [partner_own] + partner_fetched
        if d >= 1:
            tiles, mirrors[d - 1] = lax.optimization_barrier((tiles, mirrors[d - 1]))
        summed = jnp.zeros((row_height, col_width), jnp.float32)
        for tile, factor in zip(tiles, factors):
            summed = summed + jnp.dot(tile, factor, preferred_element_type=jnp.float32)
        products.append(summed)
        mirrored = lax.ppermute(summed, ("row", "col"), pairs)
        mirrors.append(mirrored)
        mirrored = mirrored.T
        bracket = summed + mirrored
        chosen = jnp.where(squared[d], bracket, 2.0 * own.astype(jnp.float32) - bracket)
        outs.append(chosen)
    chosen = jnp.stack(outs)
    return mask_blocks(chosen, own_occ).astype(jnp.bfloat16)


def solution(mesh):
    in_specs = (P(), P(), P(), P("col", None), P(None, "row", "col"))
    out_specs = P(None, "row", "col")
    return jax.shard_map(body, mesh=mesh, in_specs=in_specs, out_specs=out_specs, check_vma=False)
```
